1024 devices in a mesh: grp: 16 (over z, y_lo), mem: 64 (over x, y_hi, core).
Axes of the slice: x: 8, y: 8 (y_hi: 4, y_lo: 2; y = y_hi * 2 + y_lo), z: 8, core: 2. Of those that a mesh axis runs over, the one named last changes fastest.
Arguments:
- act: bfloat16 [3, 524288, 768], P(None, ('grp', 'mem')), may hold values from -6 to 6
- cot: bfloat16 [3, 524288, 192], P(None, ('grp', 'mem')), may hold values from -0.032958984 to 0.032958984
- owner: int32 [16, 3], P('grp'), may hold values from 0 to 63, as said below
- a_inverse: bfloat16 [64, 768, 768], P('mem'), as said below
- g_inverse: bfloat16 [64, 192, 192], P('mem'), as said below
Outputs:
- preconditioned: bfloat16 [3, 192, 768], P(None, None, 'mem')
The draws below stay inside these ranges and needn't reach their ends.
Inputs may be any that keep to these rules, and one draw needn't show every extreme that they name: Each row of owner names 3 different members. `a_inverse`: each held factor is a dense symmetric matrix: a diagonal between 0.5 and 2 plus symmetric off-diagonal entries of scale about 0.5 / sqrt(order); not necessarily definite. `g_inverse`: each held factor is a dense symmetric matrix: a diagonal between 0.5 and 2 plus symmetric off-diagonal entries of scale about 0.5 / sqrt(order); not necessarily definite.
All inputs are finite; a program needn't handle non-finite values.
Results may differ from the reference program's by a relative error of at most 0.0058.
Values may be sent and summed in bfloat16 or wider, within the bound.
No kernel may reach another device: no remote copies, remote signals or barrier semaphores. Data moves between devices by JAX's collectives and lax.ppermute only.
A program may use at most 32 MiB of HBM per device.

```python
import jax
import jax.numpy as jnp

DIM = 192
HID = 768
NL = 3
GROUPS = 16
MEMBERS = 64
SPAN = 32768
TOKENS = 524288


def held_factor(key, count, order):
    first, second = jax.random.split(key)
    diagonal = jnp.exp(jax.random.uniform(first, (count, order), jnp.float32, jnp.log(0.5), jnp.log(2.0)))
    noise = jax.random.normal(second, (count, order, order), jnp.float32)
    noise = (noise + jnp.swapaxes(noise, 1, 2)) * (0.5 / jnp.sqrt(2.0 * order))
    return (noise + jnp.eye(order, dtype=jnp.float32)[None] * diagonal[:, :, None]).astype(jnp.bfloat16)


def draw_a_inverse(key, part):
    return held_factor(jax.random.fold_in(key, 11), MEMBERS, HID)


def draw_g_inverse(key, part):
    return held_factor(jax.random.fold_in(key, 23), MEMBERS, DIM)


def draw_owner(key, part):
    keys = jax.random.split(jax.random.fold_in(key, 37), GROUPS)
    orders = jax.vmap(lambda one: jax.random.permutation(one, MEMBERS))(keys)
    table = orders[:, :NL].astype(jnp.int32)
    first_row = table[0]
    top_member = jnp.int32(MEMBERS - 1)
    has_top = jnp.any(first_row == top_member)
    first_row = jnp.where(has_top, first_row, first_row.at[0].set(top_member))
    has_zero = jnp.any(first_row == 0)
    spot = jnp.where(first_row[NL - 1] == top_member, NL - 2, NL - 1)
    places = jnp.arange(NL, dtype=jnp.int32)
    replaced = jnp.where(places == spot, jnp.int32(0), first_row)
    first_row = jnp.where(has_zero, first_row, replaced)
    return table.at[0].set(first_row).astype(jnp.int32)


def levels(key, extent, shards, least, largest):
    def one(dim, blocks):
        heights = jax.random.uniform(jax.random.fold_in(jax.random.fold_in(key, 6), dim), (blocks,), jnp.float32, least / len(shards), largest / len(shards))
        return jnp.repeat(jnp.exp(heights), extent[dim] // blocks).reshape((-1,) + (1,) * (len(extent) - dim - 1))

    level = one(*shards[0])
    for cut in shards[1:]:
        level = level * one(*cut)
    return level


def scatter_about(key, shape, scale, bound, cuts=(), kind=jnp.bfloat16):
    entries = scale * jax.random.normal(key, shape, jnp.float32)
    if cuts:
        entries = entries * levels(key, shape, cuts, -0.22, 0.18)
    return jnp.clip(entries, -bound, bound).astype(kind)


def setup_inputs(seed: int = 0) -> dict:
    key_of = jax.random.split(jax.random.key(seed), 6)
    return {
        "act": scatter_about(key_of[0], (NL, TOKENS, HID), 1.0, 6.0, ((1, 1024),)),
        "cot": scatter_about(key_of[1], (NL, TOKENS, DIM), (SPAN ** -0.5), 0.032958984, ((1, 1024),)),
        "owner": draw_owner(jax.random.fold_in(key_of[5], 71), 0),
        "a_inverse": draw_a_inverse(jax.random.fold_in(key_of[5], 71), 0),
        "g_inverse": draw_g_inverse(jax.random.fold_in(key_of[5], 71), 0),
    }


def reference(act, cot, owner, a_inverse, g_inverse):
    total = jnp.zeros((NL, DIM, HID), jnp.float32)
    for group in range(GROUPS):
        for layer in range(NL):
            inputs = act[layer, group * SPAN:(group + 1) * SPAN]
            grads = cot[layer, group * SPAN:(group + 1) * SPAN]
            summed = jnp.dot(grads.T, inputs, preferred_element_type=jnp.float32).astype(jnp.bfloat16)
            holder = owner[group, layer]
            left = jnp.dot(g_inverse[holder], summed, preferred_element_type=jnp.float32).astype(jnp.bfloat16)
            total = total.at[layer].add(jnp.dot(left, a_inverse[holder], preferred_element_type=jnp.float32))
    return total.astype(jnp.bfloat16)
```

```python
import jax
import jax.numpy as jnp
from jax import lax
from jax.sharding import PartitionSpec as P


def shards(act, cot, owner, a_inverse, g_inverse):
    layers, rows, hid = act.shape
    dim = cot.shape[2]
    members = lax.axis_size("mem")
    width = hid // members
    member = lax.axis_index("mem")
    blocks = act.reshape(layers, rows, members, width)
    local = jnp.einsum("lrd,lrmc->mldc", cot, blocks, preferred_element_type=jnp.float32)
    parts = lax.all_to_all(local, "mem", 0, 0, tiled=True)
    shard = jnp.sum(parts, axis=0).astype(jnp.bfloat16)
    slots = lax.broadcasted_iota(jnp.int32, (members, 1, 1), 0)
    outgoing = jnp.zeros((members, dim, width), jnp.bfloat16)
    for layer in range(layers):
        outgoing = jnp.where(slots == owner[0, layer], shard[layer][None], outgoing)
    gathered = lax.all_to_all(outgoing, "mem", 0, 0, tiled=True)
    grad = jnp.transpose(gathered, (1, 0, 2)).reshape(dim, hid)
    left = jnp.dot(g_inverse[0], grad, preferred_element_type=jnp.float32).astype(jnp.bfloat16)
    term = jnp.dot(left, a_inverse[0], preferred_element_type=jnp.float32)
    pieces = jnp.transpose(term.reshape(dim, members, width), (1, 0, 2))
    returned = lax.all_to_all(pieces, "mem", 0, 0, tiled=True)
    mine = jnp.stack([returned[owner[0, layer]] for layer in range(layers)])
    total = lax.psum(mine, "grp")
    return total.astype(jnp.bfloat16)


def solution(mesh):
    in_specs = (
        P(None, ("grp", "mem"), None),
        P(None, ("grp", "mem"), None),
        P("grp", None),
        P("mem", None, None),
        P("mem", None, None),
    )
    out_specs = P(None, None, "mem")
    return jax.shard_map(shards, mesh=mesh, in_specs=in_specs, out_specs=out_specs, check_vma=False)
```

```python
import jax
import jax.numpy as jnp
from jax import lax
from jax.sharding import PartitionSpec as P


def shards(act, cot, owner, a_inverse, g_inverse):
    layers, rows, hid = act.shape
    dim = cot.shape[2]
    members = lax.axis_size("mem")
    width = hid // members
    member = lax.axis_index("mem")
    blocks = act.reshape(layers, rows, members, width)
    local = jnp.einsum("lrd,lrmc->mldc", cot, blocks, preferred_element_type=jnp.float32)
    parts = lax.all_to_all(local.astype(jnp.bfloat16), "mem", 0, 0, tiled=True)
    shard = jnp.sum(parts, axis=0, dtype=jnp.float32).astype(jnp.bfloat16)
    slots = lax.broadcasted_iota(jnp.int32, (members, 1, 1), 0)
    outgoing = jnp.zeros((members, dim, width), jnp.bfloat16)
    for layer in range(layers):
        outgoing = jnp.where(slots == owner[0, layer], shard[layer][None], outgoing)
    gathered = lax.all_to_all(outgoing, "mem", 0, 0, tiled=True)
    grad = jnp.transpose(gathered, (1, 0, 2)).reshape(dim, hid)
    left = jnp.dot(g_inverse[0], grad, preferred_element_type=jnp.float32).astype(jnp.bfloat16)
    term = jnp.dot(left, a_inverse[0], preferred_element_type=jnp.float32)
    pieces = jnp.transpose(term.reshape(dim, members, width), (1, 0, 2))
    returned = lax.all_to_all(pieces, "mem", 0, 0, tiled=True)
    mine = jnp.stack([returned[owner[0, layer]] for layer in range(layers)])
    groups = lax.axis_size("grp")
    total = mine
    step = 1
    while step < groups:
        pairs = [(i, i ^ step) for i in range(groups)]
        total = total + lax.ppermute(total, "grp", pairs)
        step *= 2
    return total.astype(jnp.bfloat16)


def solution(mesh):
    in_specs = (
        P(None, ("grp", "mem"), None),
        P(None, ("grp", "mem"), None),
        P("grp", None),
        P("mem", None, None),
        P("mem", None, None),
    )
    out_specs = P(None, None, "mem")
    return jax.shard_map(shards, mesh=mesh, in_specs=in_specs, out_specs=out_specs, check_vma=False)
```

```python
import jax
import jax.numpy as jnp
from jax import lax
from jax.sharding import Mesh
from jax.sharding import PartitionSpec as P

MEM = ("x", "yh", "core")
CHIPS = ("x", "yh")


def shards(act, cot, owner, a_inverse, g_inverse):
    layers, rows, hid = act.shape
    dim = cot.shape[2]
    members = lax.axis_size(MEM)
    cores = lax.axis_size("core")
    width = hid // members
    member = lax.axis_index(MEM)
    core = lax.axis_index("core")
    blocks = act.reshape(layers, rows, members, width)
    local = jnp.einsum("lrd,lrmc->mldc", cot, blocks, preferred_element_type=jnp.float32)
    local = local.reshape(members // cores, cores, layers, dim, width)
    keep = jnp.where(core == 0, local[:, 0], local[:, 1])
    send = jnp.where(core == 0, local[:, 1], local[:, 0])
    pair = keep + lax.ppermute(send, "core", [(0, 1), (1, 0)])
    parts = lax.all_to_all(pair, CHIPS, 0, 0, tiled=True)
    shard = jnp.sum(parts, axis=0).astype(jnp.bfloat16)
    slots = lax.broadcasted_iota(jnp.int32, (members, 1, 1), 0)
    outgoing = jnp.zeros((members, dim, width), jnp.bfloat16)
    for layer in range(layers):
        outgoing = jnp.where(slots == owner[0, layer], shard[layer][None], outgoing)
    gathered = lax.all_to_all(outgoing, MEM, 0, 0, tiled=True)
    grad = jnp.transpose(gathered, (1, 0, 2)).reshape(dim, hid)
    left = jnp.dot(g_inverse[0], grad, preferred_element_type=jnp.float32).astype(jnp.bfloat16)
    term = jnp.dot(left, a_inverse[0], preferred_element_type=jnp.float32)
    pieces = jnp.transpose(term.reshape(dim, members, width), (1, 0, 2))
    returned = lax.all_to_all(pieces, MEM, 0, 0, tiled=True)
    mine = jnp.stack([returned[owner[0, layer]] for layer in range(layers)])
    groups = lax.axis_size("grp")
    total = mine
    step = 1
    while step < groups:
        pairs = [(i, i ^ step) for i in range(groups)]
        total = total + lax.ppermute(total, "grp", pairs)
        step *= 2
    return total.astype(jnp.bfloat16)


def solution(mesh):
    chips = mesh.shape["mem"] // 2
    sizes = (mesh.shape["grp"], chips // 4, 4, 2)
    fine = Mesh(mesh.devices.reshape(sizes), ("grp",) + MEM)
    in_specs = (
        P(None, ("grp",) + MEM, None),
        P(None, ("grp",) + MEM, None),
        P("grp", None),
        P(MEM, None, None),
        P(MEM, None, None),
    )
    out_specs = P(None, None, MEM)
    return jax.shard_map(shards, mesh=fine, in_specs=in_specs, out_specs=out_specs, check_vma=False)
```

```python
import jax
import jax.numpy as jnp
from jax import lax
from jax.sharding import Mesh
from jax.sharding import PartitionSpec as P

MEM = ("x", "yh", "core")
CHIPS = ("x", "yh")


def shards(act, cot, owner, a_inverse, g_inverse):
    layers, rows, hid = act.shape
    dim = cot.shape[2]
    members = lax.axis_size(MEM)
    cores = lax.axis_size("core")
    width = hid // members
    member = lax.axis_index(MEM)
    core = lax.axis_index("core")
    blocks = act.reshape(layers, rows, members // cores, cores, width)
    mine_cols = lax.dynamic_index_in_dim(blocks, core, 3, keepdims=False)
    other_cols = lax.dynamic_index_in_dim(blocks, 1 - core, 3, keepdims=False)
    keep = jnp.einsum("lrd,lrmc->mldc", cot, mine_cols, preferred_element_type=jnp.float32)
    send = jnp.einsum("lrd,lrmc->mldc", cot, other_cols, preferred_element_type=jnp.float32)
    pair = keep + lax.ppermute(send, "core", [(0, 1), (1, 0)])
    parts = lax.all_to_all(pair, CHIPS, 0, 0, tiled=True)
    shard = jnp.sum(parts, axis=0).astype(jnp.bfloat16)
    slots = lax.broadcasted_iota(jnp.int32, (members, 1, 1), 0)
    outgoing = jnp.zeros((members, dim, width), jnp.bfloat16)
    for layer in range(layers):
        outgoing = jnp.where(slots == owner[0, layer], shard[layer][None], outgoing)
    gathered = lax.all_to_all(outgoing, MEM, 0, 0, tiled=True)
    grad = jnp.transpose(gathered, (1, 0, 2)).reshape(dim, hid)
    left = jnp.dot(g_inverse[0], grad, preferred_element_type=jnp.float32).astype(jnp.bfloat16)
    term = jnp.dot(left, a_inverse[0], preferred_element_type=jnp.float32)
    pieces = jnp.transpose(term.reshape(dim, members, width), (1, 0, 2))
    returned = lax.all_to_all(pieces, MEM, 0, 0, tiled=True)
    mine = jnp.stack([returned[owner[0, layer]] for layer in range(layers)])
    groups = lax.axis_size("grp")
    total = mine
    step = 1
    while step < groups:
        pairs = [(i, i ^ step) for i in range(groups)]
        total = total + lax.ppermute(total, "grp", pairs)
        step *= 2
    return total.astype(jnp.bfloat16)


def solution(mesh):
    chips = mesh.shape["mem"] // 2
    sizes = (mesh.shape["grp"], chips // 4, 4, 2)
    fine = Mesh(mesh.devices.reshape(sizes), ("grp",) + MEM)
    in_specs = (
        P(None, ("grp",) + MEM, None),
        P(None, ("grp",) + MEM, None),
        P("grp", None),
        P(MEM, None, None),
        P(MEM, None, None),
    )
    out_specs = P(None, None, MEM)
    return jax.shard_map(shards, mesh=fine, in_specs=in_specs, out_specs=out_specs, check_vma=False)
```

```python
import jax
import jax.numpy as jnp
from jax import lax
from jax.sharding import Mesh
from jax.sharding import PartitionSpec as P

MEM = ("x", "yh", "core")
CHIPS = ("x", "yh")


def shards(act, cot, owner, a_inverse, g_inverse):
    layers, rows, hid = act.shape
    dim = cot.shape[2]
    members = lax.axis_size(MEM)
    cores = lax.axis_size("core")
    width = hid // members
    member = lax.axis_index(MEM)
    core = lax.axis_index("core")
    height = dim // members
    blocks = cot.reshape(layers, rows, members // cores, cores, height)
    mine_rows = lax.dynamic_index_in_dim(blocks, core, 3, keepdims=False)
    other_rows = lax.dynamic_index_in_dim(blocks, 1 - core, 3, keepdims=False)
    keep = jnp.einsum("lrmk,lrh->mlkh", mine_rows, act, preferred_element_type=jnp.float32)
    send = jnp.einsum("lrmk,lrh->mlkh", other_rows, act, preferred_element_type=jnp.float32)
    pair = keep + lax.ppermute(send, "core", [(0, 1), (1, 0)])
    parts = lax.all_to_all(pair, CHIPS, 0, 0, tiled=True)
    shard = jnp.sum(parts, axis=0).astype(jnp.bfloat16)
    slots = lax.broadcasted_iota(jnp.int32, (members, 1, 1), 0)
    outgoing = jnp.zeros((members, height, hid), jnp.bfloat16)
    for layer in range(layers):
        outgoing = jnp.where(slots == owner[0, layer], shard[layer][None], outgoing)
    gathered = lax.all_to_all(outgoing, MEM, 0, 0, tiled=True)
    grad = gathered.reshape(dim, hid)
    left = jnp.dot(g_inverse[0], grad, preferred_element_type=jnp.float32).astype(jnp.bfloat16)
    term = jnp.dot(left, a_inverse[0], preferred_element_type=jnp.float32)
    pieces = jnp.transpose(term.reshape(dim, members, width), (1, 0, 2))
    returned = lax.all_to_all(pieces, MEM, 0, 0, tiled=True)
    mine = jnp.stack([returned[owner[0, layer]] for layer in range(layers)])
    groups = lax.axis_size("grp")
    total = mine
    step = 1
    while step < groups:
        pairs = [(i, i ^ step) for i in range(groups)]
        total = total + lax.ppermute(total, "grp", pairs)
        step *= 2
    return total.astype(jnp.bfloat16)


def solution(mesh):
    chips = mesh.shape["mem"] // 2
    sizes = (mesh.shape["grp"], chips // 4, 4, 2)
    fine = Mesh(mesh.devices.reshape(sizes), ("grp",) + MEM)
    in_specs = (
        P(None, ("grp",) + MEM, None),
        P(None, ("grp",) + MEM, None),
        P("grp", None),
        P(MEM, None, None),
        P(MEM, None, None),
    )
    out_specs = P(None, None, MEM)
    return jax.shard_map(shards, mesh=fine, in_specs=in_specs, out_specs=out_specs, check_vma=False)
```

```python
import jax
import jax.numpy as jnp
from jax import lax
from jax.sharding import Mesh
from jax.sharding import PartitionSpec as P

MEM = ("x", "yh", "core")
CHIPS = ("x", "yh")


def shards(act, cot, owner, a_inverse, g_inverse):
    layers, rows, hid = act.shape
    dim = cot.shape[2]
    members = lax.axis_size(MEM)
    cores = lax.axis_size("core")
    width = hid // members
    member = lax.axis_index(MEM)
    core = lax.axis_index("core")
    height = dim // members
    blocks = cot.reshape(layers, rows, members // cores, cores, height)
    mine_rows = lax.dynamic_index_in_dim(blocks, core, 3, keepdims=False)
    other_rows = lax.dynamic_index_in_dim(blocks, 1 - core, 3, keepdims=False)
    keep = jnp.einsum("lrmk,lrh->mlkh", mine_rows, act, preferred_element_type=jnp.float32)
    send = jnp.einsum("lrmk,lrh->mlkh", other_rows, act, preferred_element_type=jnp.float32)
    pair = keep + lax.ppermute(send, "core", [(0, 1), (1, 0)])
    parts = lax.all_to_all(pair, CHIPS, 0, 0, tiled=True)
    shard = jnp.sum(parts, axis=0).astype(jnp.bfloat16)
    slots = lax.broadcasted_iota(jnp.int32, (members, 1, 1), 0)
    outgoing = jnp.zeros((members, height, hid), jnp.bfloat16)
    for layer in range(layers):
        outgoing = jnp.where(slots == owner[0, layer], shard[layer][None], outgoing)
    gathered = lax.all_to_all(outgoing, MEM, 0, 0, tiled=True)
    grad = gathered.reshape(dim, hid)
    left = jnp.dot(g_inverse[0], grad, preferred_element_type=jnp.float32).astype(jnp.bfloat16)
    flipped = jnp.einsum("ek,kh->he", left, a_inverse[0], preferred_element_type=jnp.float32)
    pieces = flipped.reshape(members, width, dim)
    returned = lax.all_to_all(pieces, MEM, 0, 0, tiled=True)
    mine = jnp.stack([returned[owner[0, layer]] for layer in range(layers)])
    groups = lax.axis_size("grp")
    total = mine
    step = groups // 2
    while step >= 1:
        pairs = [(i, i ^ step) for i in range(groups)]
        total = total + lax.ppermute(total, "grp", pairs)
        step //= 2
    return jnp.transpose(total, (0, 2, 1)).astype(jnp.bfloat16)


def solution(mesh):
    chips = mesh.shape["mem"] // 2
    sizes = (mesh.shape["grp"], chips // 4, 4, 2)
    fine = Mesh(mesh.devices.reshape(sizes), ("grp",) + MEM)
    in_specs = (
        P(None, ("grp",) + MEM, None),
        P(None, ("grp",) + MEM, None),
        P("grp", None),
        P(MEM, None, None),
        P(MEM, None, None),
    )
    out_specs = P(None, None, MEM)
    return jax.shard_map(shards, mesh=fine, in_specs=in_specs, out_specs=out_specs, check_vma=False)
```

```python
import jax
import jax.numpy as jnp
from jax import lax
from jax.sharding import Mesh
from jax.sharding import PartitionSpec as P

MEM = ("x", "yh", "core")
CHIPS = ("x", "yh")


def shards(act, cot, owner, a_inverse, g_inverse):
    layers, rows, hid = act.shape
    dim = cot.shape[2]
    members = lax.axis_size(MEM)
    cores = lax.axis_size("core")
    width = hid // members
    member = lax.axis_index(MEM)
    core = lax.axis_index("core")
    height = dim // members
    blocks = cot.reshape(layers, rows, members // cores, cores, height)
    mine_rows = lax.dynamic_index_in_dim(blocks, core, 3, keepdims=False)
    other_rows = lax.dynamic_index_in_dim(blocks, 1 - core, 3, keepdims=False)
    keep = jnp.einsum("lrmk,lrh->mlkh", mine_rows, act, preferred_element_type=jnp.float32)
    send = jnp.einsum("lrmk,lrh->mlkh", other_rows, act, preferred_element_type=jnp.float32)
    pair = keep + lax.ppermute(send, "core", [(0, 1), (1, 0)])
    parts = lax.all_to_all(pair, CHIPS, 0, 0, tiled=True)
    shard = jnp.sum(parts, axis=0).astype(jnp.bfloat16)
    slots = lax.broadcasted_iota(jnp.int32, (members, layers), 0)
    route = (slots == owner[0][None, :]).astype(jnp.bfloat16)
    outgoing = jnp.einsum("jl,lkh->jkh", route, shard, preferred_element_type=jnp.float32)
    outgoing = outgoing.astype(jnp.bfloat16)
    gathered = lax.all_to_all(outgoing, MEM, 0, 0, tiled=True)
    grad = gathered.reshape(dim, hid)
    left = jnp.dot(g_inverse[0], grad, preferred_element_type=jnp.float32).astype(jnp.bfloat16)
    flipped = jnp.einsum("ek,kh->he", left, a_inverse[0], preferred_element_type=jnp.float32)
    pieces = flipped.reshape(members, width, dim)
    returned = lax.all_to_all(pieces, MEM, 0, 0, tiled=True)
    mine = jnp.stack([returned[owner[0, layer]] for layer in range(layers)])
    groups = lax.axis_size("grp")
    total = mine
    step = groups // 2
    while step >= 1:
        pairs = [(i, i ^ step) for i in range(groups)]
        total = total + lax.ppermute(total, "grp", pairs)
        step //= 2
    return jnp.transpose(total, (0, 2, 1)).astype(jnp.bfloat16)


def solution(mesh):
    chips = mesh.shape["mem"] // 2
    sizes = (mesh.shape["grp"], chips // 4, 4, 2)
    fine = Mesh(mesh.devices.reshape(sizes), ("grp",) + MEM)
    in_specs = (
        P(None, ("grp",) + MEM, None),
        P(None, ("grp",) + MEM, None),
        P("grp", None),
        P(MEM, None, None),
        P(MEM, None, None),
    )
    out_specs = P(None, None, MEM)
    return jax.shard_map(shards, mesh=fine, in_specs=in_specs, out_specs=out_specs, check_vma=False)
```

```python
import jax
import jax.numpy as jnp
from jax import lax
from jax.sharding import Mesh
from jax.sharding import PartitionSpec as P

MEM = ("x", "yh", "core")
CHIPS = ("x", "yh")


def shards(act, cot, owner, a_inverse, g_inverse):
    layers, rows, hid = act.shape
    dim = cot.shape[2]
    members = lax.axis_size(MEM)
    cores = lax.axis_size("core")
    width = hid // members
    member = lax.axis_index(MEM)
    core = lax.axis_index("core")
    height = dim // members
    blocks = cot.reshape(layers, rows, members // cores, cores, height)
    mine_rows = lax.dynamic_index_in_dim(blocks, core, 3, keepdims=False)
    other_rows = lax.dynamic_index_in_dim(blocks, 1 - core, 3, keepdims=False)
    keep = jnp.einsum("lrmk,lrh->mklh", mine_rows, act, preferred_element_type=jnp.float32)
    send = jnp.einsum("lrmk,lrh->mklh", other_rows, act, preferred_element_type=jnp.float32)
    pair = keep + lax.ppermute(send, "core", [(0, 1), (1, 0)])
    parts = lax.all_to_all(pair, CHIPS, 0, 0, tiled=True)
    shard = jnp.transpose(jnp.sum(parts, axis=0), (1, 0, 2)).astype(jnp.bfloat16)
    slots = lax.broadcasted_iota(jnp.int32, (members, layers), 0)
    route = (slots == owner[0][None, :]).astype(jnp.bfloat16)
    outgoing = jnp.einsum("jl,lkh->jkh", route, shard, preferred_element_type=jnp.float32)
    outgoing = outgoing.astype(jnp.bfloat16)
    gathered = lax.all_to_all(outgoing, MEM, 0, 0, tiled=True)
    grad = gathered.reshape(dim, hid)
    left = jnp.dot(g_inverse[0], grad, preferred_element_type=jnp.float32).astype(jnp.bfloat16)
    flipped = jnp.einsum("ek,kh->he", left, a_inverse[0], preferred_element_type=jnp.float32)
    pieces = flipped.reshape(members, width, dim)
    returned = lax.all_to_all(pieces, MEM, 0, 0, tiled=True)
    mine = jnp.stack([returned[owner[0, layer]] for layer in range(layers)])
    groups = lax.axis_size("grp")
    total = mine
    step = groups // 2
    while step >= 1:
        pairs = [(i, i ^ step) for i in range(groups)]
        total = total + lax.ppermute(total, "grp", pairs)
        step //= 2
    return jnp.transpose(total, (0, 2, 1)).astype(jnp.bfloat16)


def solution(mesh):
    chips = mesh.shape["mem"] // 2
    sizes = (mesh.shape["grp"], chips // 4, 4, 2)
    fine = Mesh(mesh.devices.reshape(sizes), ("grp",) + MEM)
    in_specs = (
        P(None, ("grp",) + MEM, None),
        P(None, ("grp",) + MEM, None),
        P("grp", None),
        P(MEM, None, None),
        P(MEM, None, None),
    )
    out_specs = P(None, None, MEM)
    return jax.shard_map(shards, mesh=fine, in_specs=in_specs, out_specs=out_specs, check_vma=False)
```
